128 devices in a mesh: half: 2 (over y_hi), tile: 64 (over x, y_lo, z, core).
Axes of the slice: x: 4, y: 4 (y_hi: 2, y_lo: 2; y = y_hi * 2 + y_lo), z: 4, core: 2. Of those that a mesh axis runs over, the one named last changes fastest.
Arguments:
- innov: bfloat16 [2, 1048576, 128], P('half', 'tile'), may hold values from -6 to 6
- pred: bfloat16 [2, 1048576, 128], P('half', 'tile'), may hold values from -0.59765625 to 0.59765625
- obs_weight: float32 [1048576], P('tile'), may hold values from 0.4 to 4
- owner: int32 [8192, 1], P('tile'), may hold values from 0 to 63; in each aligned block of 128 rows (0 to 127, 128 to 255, ...) at most 4 rows name the same one
- counts: int32 [64], P('tile'), may hold values from 64 to 128
- neighbours: int32 [64, 9], P('tile'), may hold values from 0 to 63, as said below
- loc_weight: float32 [64, 9], P('tile'), may hold values from 0.3 to 1
- ensemble: bfloat16 [2, 1048576, 128], P('half', 'tile'), may hold values from -6 to 6
Outputs:
- analysis: bfloat16 [2, 1048576, 128], P('half', 'tile')
The draws below stay inside these ranges and needn't reach their ends.
Inputs may be any that keep to these rules, and one draw needn't show every extreme that they name: Of the 128 blocks of one tile at most 4 have the same owner, and some tile gives exactly 4 blocks to one owner; every tile owns some block. `neighbours`: each row names 9 different tiles, the first one being the row's own tile.
All inputs are finite; a program needn't handle non-finite values.
Results may differ from the reference program's by a relative error of at most 0.0072.
Values may be sent and summed in bfloat16 or wider, within the bound.
No kernel may reach another device: no remote copies, remote signals or barrier semaphores. Data moves between devices by JAX's collectives and lax.ppermute only.
A program may use at most 128 MiB of HBM per device.

```python
import math
import jax
import jax.numpy as jnp
import numpy as np
from jax import lax

MEMBERS = 128
BLOCK = 128
NBR = 9
BLK_DEV = 128
S_DEV = 16384
TILES = 64
SLOT = 4
OBS = 1048576
BLOCKS = 8192
STATE = 1048576


def draw_neighbours(key, part):
    keys = jax.random.split(jax.random.fold_in(key, 7), TILES)

    def one_row(row_key, tile_id):
        others = jax.random.permutation(row_key, TILES - 1)[:NBR - 1].astype(jnp.int32)
        return jnp.concatenate([tile_id[None], (tile_id + 1 + others) % TILES]).astype(jnp.int32)
    return jax.vmap(one_row)(keys, jnp.arange(TILES, dtype=jnp.int32))


def set_ends(values, stream_key, smallest, top_value):
    extent = values.shape
    place = [jax.random.randint(jax.random.fold_in(stream_key, axis), (), 0, extent[axis]) for axis in range(len(extent))]
    values = values.at[tuple(place)].set(smallest)
    longest = extent.index(max(extent))
    place[longest] = (place[longest] + 1) % extent[longest]
    return values.at[tuple(place)].set(top_value)


def shard_levels(key, shape, pieces, smallest, top_value):
    def one(axis_at, parts):
        steps = jax.random.uniform(jax.random.fold_in(jax.random.fold_in(key, 6), axis_at), (parts,), jnp.float32, smallest / len(pieces), top_value / len(pieces))
        return jnp.repeat(jnp.exp(steps), shape[axis_at] // parts).reshape((-1,) + (1,) * (len(shape) - axis_at - 1))

    level = one(*pieces[0])
    for cut in pieces[1:]:
        level = level * one(*cut)
    return level


def routed_block(stream_key, own, number, rows, count, top, most, slope):
    sequence = jax.random.permutation(stream_key, count)
    heavy_load, usual = portions_of(count, rows * top, most, slope, True), portions_of(count, rows * top, most, slope, False)
    places = jnp.arange(count)

    def named(tallies, turn):
        used = int((tallies > 0).sum())
        fixed = max(1, used // 4)
        moved = fixed + (places - fixed + turn * (used - fixed)) % max(1, count - fixed)
        return jnp.zeros((count,), jnp.int32).at[sequence[jnp.where(places < fixed, places, moved)]].set(jnp.asarray(tallies, jnp.int32))

    tallies = jnp.where(number % 4 == 0, named(heavy_load, number // 4), named(usual, number - number // 4 - 1))
    mixed = jax.random.permutation(jax.random.fold_in(own, 3), count)
    source_of, taker = mixed[0:count // 2 * 2:2], mixed[1:count // 2 * 2:2]
    slack = jnp.minimum(tallies[source_of] - 1, most - tallies[taker]) // 2
    slack = jnp.where((source_of == sequence[0]) | (taker == sequence[0]) | (tallies[taker] == 0), 0, jnp.maximum(slack, 0))
    moved = jax.random.randint(jax.random.fold_in(own, 4), (count // 2,), 0, 1 << 20) % (slack + 1)
    tallies = tallies.at[source_of].add(-moved).at[taker].add(moved)
    labels = jnp.searchsorted(jnp.cumsum(tallies), jnp.arange(rows * top), side="right").astype(jnp.int32)
    grid = labels.reshape(top, rows).T
    grid = grid[jax.random.permutation(jax.random.fold_in(own, 1), rows)]
    turn = jax.random.randint(jax.random.fold_in(own, 2), (rows, 1), 0, top)
    return jnp.take_along_axis(grid, (jnp.arange(top)[None, :] + turn) % top, axis=1)


def portions_of(number_of, total, bound, slope, full):
    portions = [(1 << 20) // math.isqrt(rank ** slope) + 1 for rank in range(1, number_of + 1)]
    largest = bound if full else min(bound, max(-(-total // number_of), total * portions[0] // sum(portions)))
    least = 1 if total - largest >= number_of - 1 else 0
    given, surplus = [largest] + [least] * (number_of - 1), total - largest - least * (number_of - 1)
    while surplus > 0:
        movable = [i for i in range(1, number_of) if given[i] < largest] or [i for i in range(1, number_of) if given[i] < bound]
        pool, remaining = sum([portions[i] for i in movable]), surplus
        for i in movable:
            more = min(bound - given[i], max(1, remaining * portions[i] // pool), surplus)
            given[i] = given[i] + more
            surplus = surplus - more
    return np.array(given)


def normal_values(own_key, shape, deviation, limit, shards=(), kind=jnp.bfloat16):
    gain = shard_levels(own_key, shape, shards, -0.22, 0.18) if shards else 1.0
    values = jax.random.normal(own_key, shape, jnp.float32) * deviation * gain
    return jnp.minimum(jnp.maximum(values, -limit), limit).astype(kind)


def setup_inputs(seed: int = 0) -> dict:
    arg_keys = jax.random.split(jax.random.key(seed), 9)
    innov = normal_values(arg_keys[0], (2, OBS, MEMBERS), 1.0, 6.0, ((0, 2), (1, 64)))
    pred = normal_values(arg_keys[1], (2, OBS, MEMBERS), 0.1, 0.59765625, ((0, 2), (1, 64)))
    obs_weight = jnp.clip(jnp.exp(math.log(4.0) - 2.3025851 * jax.random.uniform(arg_keys[2], (OBS,), jnp.float32) ** shard_levels(arg_keys[2], (OBS,), ((0, 64),), -0.2, 0.2)), 0.4, 4.0)
    owner_keys = jax.random.split(jax.random.fold_in(arg_keys[3], 1), BLOCKS // BLK_DEV)
    owner_turns = jax.random.permutation(jax.random.fold_in(arg_keys[3], 3), BLOCKS // BLK_DEV)
    owner = jax.vmap(lambda own, number: routed_block(jax.random.fold_in(arg_keys[3], 2), own, number, BLK_DEV, TILES, 1, SLOT, 2))(owner_keys, owner_turns).reshape((BLOCKS, 1))
    counts = set_ends(jax.random.randint(arg_keys[4], (TILES,), BLK_DEV // 2, BLK_DEV + 1), jax.random.fold_in(arg_keys[4], 1), BLK_DEV // 2, BLK_DEV).astype(jnp.int32)
    neighbours = draw_neighbours(jax.random.fold_in(arg_keys[8], 71), 0)
    loc_weight = jnp.clip(0.3 + 0.7 * jax.random.uniform(arg_keys[6], (TILES, NBR), jnp.float32) ** shard_levels(arg_keys[6], (TILES, NBR), ((0, 64),), -0.2, 0.2), 0.3, 1.0)
    ensemble = normal_values(arg_keys[7], (2, STATE, MEMBERS), 1.0, 6.0, ((0, 2), (1, 64)))
    return dict(innov=innov, pred=pred, obs_weight=obs_weight, owner=owner, counts=counts, neighbours=neighbours, loc_weight=loc_weight, ensemble=ensemble)


def batch_sums(zed_own, unn_other, dest):
    zed_b = zed_own.reshape(TILES, BLK_DEV, BLOCK, MEMBERS)
    unn_b = unn_other.reshape(TILES, BLK_DEV, BLOCK, MEMBERS)
    dest_b = dest.reshape(TILES, BLK_DEV)

    def step(carry, items):
        zed_t, unn_t, dest_t = items
        zf = zed_t.astype(jnp.float32)
        uf = unn_t.astype(jnp.float32)
        gram_b = jnp.einsum('bri,brj->bij', zf, zf, precision=lax.Precision.HIGHEST)
        cross_b = jnp.einsum('bri,brj->bij', zf, uf, precision=lax.Precision.HIGHEST)
        gram_s = carry[0] + jax.ops.segment_sum(gram_b, dest_t, num_segments=TILES)
        cross_s = carry[1] + jax.ops.segment_sum(cross_b, dest_t, num_segments=TILES)
        return ((gram_s, cross_s), None)
    start = (jnp.zeros((TILES, MEMBERS, MEMBERS), jnp.float32), jnp.zeros((TILES, MEMBERS, MEMBERS), jnp.float32))
    result, unused = lax.scan(step, start, (zed_b, unn_b, dest_b))
    return result

def solve_one(gram_s, cross_s):
    eye = jnp.eye(MEMBERS, dtype=jnp.float32)
    factor = jnp.linalg.cholesky((MEMBERS - 1.0) * eye + gram_s)
    return jax.scipy.linalg.cho_solve((factor, True), cross_s)

def reference(innov, pred, obs_weight, owner, counts, neighbours, loc_weight, ensemble):
    live = (jnp.arange(BLK_DEV, dtype=jnp.int32)[None, :] < counts[:, None]).astype(jnp.float32)
    row_scale = obs_weight * jnp.repeat(live.reshape(-1), BLOCK)
    zed = (pred.astype(jnp.float32) * row_scale[None, :, None]).astype(jnp.bfloat16)
    unn = (innov.astype(jnp.float32) * row_scale[None, :, None]).astype(jnp.bfloat16)
    dest = owner[:, 0]
    tile_ids = jnp.arange(TILES, dtype=jnp.int32)
    loc = jnp.sum(loc_weight[:, :, None] * (neighbours[:, :, None] == tile_ids[None, None, :]).astype(jnp.float32), axis=1)
    outputs = []
    spreads = []
    anoms = []
    for half_index in range(2):
        other = 1 - half_index
        gram_s, cross_s = batch_sums(zed[half_index], unn[other], dest)
        weights = jax.vmap(solve_one)(gram_s, cross_s)
        spread = jnp.einsum('sn,sij->nij', loc, weights, precision=lax.Precision.HIGHEST).astype(jnp.bfloat16)
        spreads.append(spread)
        ens_f = ensemble[half_index].astype(jnp.float32)
        center = jnp.mean(ens_f, axis=1, keepdims=True)
        anoms.append((ens_f - center).astype(jnp.bfloat16).reshape(TILES, S_DEV, MEMBERS))
    for half_index in range(2):
        other = 1 - half_index

        def tile_incr(pair):
            return jnp.dot(pair[0].astype(jnp.float32), pair[1].astype(jnp.float32), preferred_element_type=jnp.float32).astype(jnp.bfloat16)
        incr = lax.map(tile_incr, (anoms[half_index], spreads[half_index])).reshape(STATE, MEMBERS)
        outputs.append((ensemble[other].astype(jnp.float32) + incr.astype(jnp.float32)).astype(jnp.bfloat16))
    analysis_lo = outputs[1]
    analysis_hi = outputs[0]
    return jnp.stack([analysis_lo, analysis_hi], axis=0)
```

```python
import jax
import jax.numpy as jnp
from jax import lax
from jax.sharding import PartitionSpec as P


def from_partner(block, axis, apart):
    count = lax.axis_size(axis)
    route = []
    for low in range(count):
        high = low | 1 << apart
        if high != low and high < count:
            route += [(low, high), (high, low)]
    return lax.ppermute(block, axis, route)


def step(innov, pred, obs_weight, owner, counts, neighbours, loc_weight, ensemble):
    tiles = lax.axis_size("tile")
    members = pred.shape[2]
    obs_rows = pred.shape[1]
    blocks = owner.shape[0]
    block_rows = obs_rows // blocks
    slot_count = max(2, 2 * blocks // tiles)
    block_ids = jnp.arange(blocks, dtype=jnp.int32)
    live = (block_ids < counts[0]).astype(jnp.float32)
    row_scale = obs_weight * jnp.repeat(live, block_rows)
    zed = (pred[0].astype(jnp.float32) * row_scale[:, None]).astype(jnp.bfloat16)
    unn = (innov[0].astype(jnp.float32) * row_scale[:, None]).astype(jnp.bfloat16)
    partner = from_partner(unn, "half", 0)
    ens_f = ensemble[0].astype(jnp.float32)
    center = jnp.mean(ens_f, axis=1, keepdims=True)
    anomalies = (ens_f - center).astype(jnp.bfloat16)
    anomalies, partner = lax.optimization_barrier((anomalies, partner))
    partner_anom = from_partner(anomalies, "half", 0)

    dest = owner[:, 0]
    zed_b = zed.reshape(blocks, block_rows, members)
    partner_b = partner.reshape(blocks, block_rows, members)
    same = (dest[None, :] == dest[:, None]) & (block_ids[None, :] < block_ids[:, None])
    rank = jnp.sum(same.astype(jnp.int32), axis=1)
    position = dest * slot_count + rank
    slot_ids = jnp.arange(tiles * slot_count, dtype=jnp.int32)
    hit = position[None, :] == slot_ids[:, None]
    source = jnp.sum(hit.astype(jnp.int32) * block_ids[None, :], axis=1)
    filled = jnp.any(hit, axis=1)
    slot_zed = jnp.where(filled[:, None, None], zed_b[source], jnp.zeros((), jnp.bfloat16))
    slot_zed = slot_zed.reshape(tiles, slot_count * block_rows, members)
    slot_unn = jnp.where(filled[:, None, None], partner_b[source], jnp.zeros((), jnp.bfloat16))
    slot_unn = slot_unn.reshape(tiles, slot_count * block_rows, members)
    dims = (((1,), (1,)), ((0,), (0,)))
    gram_part = lax.dot_general(slot_zed, slot_zed, dims, preferred_element_type=jnp.float32)
    gram_got = lax.all_to_all(gram_part, "tile", 0, 0, tiled=True)
    gram = jnp.sum(gram_got, axis=0)
    cross_part = lax.dot_general(slot_zed, slot_unn, dims, preferred_element_type=jnp.float32)
    cross = jnp.sum(lax.all_to_all(cross_part, "tile", 0, 0, tiled=True), axis=0)
    eye = jnp.eye(members, dtype=jnp.float32)
    factor = jnp.linalg.cholesky((members - 1.0) * eye + gram)
    weights = jax.scipy.linalg.cho_solve((factor, True), cross)
    tile_ids = jnp.arange(tiles, dtype=jnp.int32)
    loc_row = jnp.sum(
        loc_weight[0][:, None] * (neighbours[0][:, None] == tile_ids[None, :]).astype(jnp.float32),
        axis=0,
    )
    reach = loc_row[:, None, None] * weights[None, :, :]
    spread = jnp.sum(lax.all_to_all(reach, "tile", 0, 0, tiled=True), axis=0).astype(jnp.bfloat16)
    partner_spread = from_partner(spread, "half", 0)
    incr = jnp.dot(partner_anom, partner_spread, preferred_element_type=jnp.float32).astype(jnp.bfloat16)
    analysis = (ens_f + incr.astype(jnp.float32)).astype(jnp.bfloat16)
    return analysis[None]


def solution(mesh):
    return jax.shard_map(
        step,
        mesh=mesh,
        in_specs=(
            P("half", "tile", None),
            P("half", "tile", None),
            P("tile"),
            P("tile", None),
            P("tile"),
            P("tile", None),
            P("tile", None),
            P("half", "tile", None),
        ),
        out_specs=P("half", "tile", None),
        check_vma=False,
    )
```

```python
import jax
import jax.numpy as jnp
from jax import lax
from jax.sharding import PartitionSpec as P


def from_partner(block, axis, apart):
    count = lax.axis_size(axis)
    route = []
    for low in range(count):
        high = low | 1 << apart
        if high != low and high < count:
            route += [(low, high), (high, low)]
    return lax.ppermute(block, axis, route)


def step(innov, pred, obs_weight, owner, counts, neighbours, loc_weight, ensemble):
    tiles = lax.axis_size("tile")
    members = pred.shape[2]
    obs_rows = pred.shape[1]
    blocks = owner.shape[0]
    block_rows = obs_rows // blocks
    slot_count = max(2, 2 * blocks // tiles)
    block_ids = jnp.arange(blocks, dtype=jnp.int32)
    live = (block_ids < counts[0]).astype(jnp.float32)
    row_scale = obs_weight * jnp.repeat(live, block_rows)
    zed = (pred[0].astype(jnp.float32) * row_scale[:, None]).astype(jnp.bfloat16)
    unn = (innov[0].astype(jnp.float32) * row_scale[:, None]).astype(jnp.bfloat16)
    partner_zed = from_partner(zed, "half", 0)

    dest = owner[:, 0]
    same = (dest[None, :] == dest[:, None]) & (block_ids[None, :] < block_ids[:, None])
    rank = jnp.sum(same.astype(jnp.int32), axis=1)
    position = dest * slot_count + rank
    slot_ids = jnp.arange(tiles * slot_count, dtype=jnp.int32)
    hit = position[None, :] == slot_ids[:, None]
    source = jnp.sum(hit.astype(jnp.int32) * block_ids[None, :], axis=1)
    filled = jnp.any(hit, axis=1)

    def slots(rows):
        got = jnp.where(filled[:, None, None], rows.reshape(blocks, block_rows, members)[source], jnp.zeros((), rows.dtype))
        return got.reshape(tiles, slot_count * block_rows, members)

    dims = (((1,), (1,)), ((0,), (0,)))
    eye = jnp.eye(members, dtype=jnp.float32)
    own_zed = slots(zed)
    gram_part = lax.dot_general(own_zed, own_zed, dims, preferred_element_type=jnp.float32)
    gram = jnp.sum(lax.all_to_all(gram_part, "tile", 0, 0, tiled=True), axis=0)
    factor = jnp.linalg.cholesky((members - 1.0) * eye + gram)
    partner_factor = from_partner(factor, "half", 0)
    ens_f = ensemble[0].astype(jnp.float32)
    center = jnp.mean(ens_f, axis=1, keepdims=True)
    anomalies = (ens_f - center).astype(jnp.bfloat16)
    anomalies, partner_zed, partner_factor = lax.optimization_barrier((anomalies, partner_zed, partner_factor))
    partner_anom = from_partner(anomalies, "half", 0)

    other_zed = slots(partner_zed)
    own_unn = slots(unn)
    cross_part = lax.dot_general(other_zed, own_unn, dims, preferred_element_type=jnp.float32)
    cross = jnp.sum(lax.all_to_all(cross_part, "tile", 0, 0, tiled=True), axis=0)
    weights = jax.scipy.linalg.cho_solve((partner_factor, True), cross)
    tile_ids = jnp.arange(tiles, dtype=jnp.int32)
    loc_row = jnp.sum(
        loc_weight[0][:, None] * (neighbours[0][:, None] == tile_ids[None, :]).astype(jnp.float32),
        axis=0,
    )
    reach = loc_row[:, None, None] * weights[None, :, :]
    spread = jnp.sum(lax.all_to_all(reach, "tile", 0, 0, tiled=True), axis=0).astype(jnp.bfloat16)
    incr = jnp.dot(partner_anom, spread, preferred_element_type=jnp.float32).astype(jnp.bfloat16)
    analysis = (ens_f + incr.astype(jnp.float32)).astype(jnp.bfloat16)
    return analysis[None]


def solution(mesh):
    return jax.shard_map(
        step,
        mesh=mesh,
        in_specs=(
            P("half", "tile", None),
            P("half", "tile", None),
            P("tile"),
            P("tile", None),
            P("tile"),
            P("tile", None),
            P("tile", None),
            P("half", "tile", None),
        ),
        out_specs=P("half", "tile", None),
        check_vma=False,
    )
```

```python
import jax
import jax.numpy as jnp
from jax import lax
from jax.sharding import PartitionSpec as P


def from_partner(block, axis, apart):
    count = lax.axis_size(axis)
    route = []
    for low in range(count):
        high = low | 1 << apart
        if high != low and high < count:
            route += [(low, high), (high, low)]
    return lax.ppermute(block, axis, route)


def step(innov, pred, obs_weight, owner, counts, neighbours, loc_weight, ensemble):
    tiles = lax.axis_size("tile")
    members = pred.shape[2]
    obs_rows = pred.shape[1]
    blocks = owner.shape[0]
    block_rows = obs_rows // blocks
    block_ids = jnp.arange(blocks, dtype=jnp.int32)
    live = (block_ids < counts[0]).astype(jnp.float32)
    row_scale = obs_weight * jnp.repeat(live, block_rows)
    zed = (pred[0].astype(jnp.float32) * row_scale[:, None]).astype(jnp.bfloat16)
    unn = (innov[0].astype(jnp.float32) * row_scale[:, None]).astype(jnp.bfloat16)
    partner_zed = from_partner(zed, "half", 0)

    dest = owner[:, 0]
    tile_ids = jnp.arange(tiles, dtype=jnp.int32)
    owned = (dest[None, :] == tile_ids[:, None]).astype(jnp.float32)

    def owner_sums(left, right):
        per_block = lax.dot_general(
            left.reshape(blocks, block_rows, members),
            right.reshape(blocks, block_rows, members),
            (((1,), (1,)), ((0,), (0,))),
            preferred_element_type=jnp.float32,
        )
        return lax.dot_general(owned, per_block, (((1,), (0,)), ((), ())), precision=lax.Precision.HIGHEST)

    eye = jnp.eye(members, dtype=jnp.float32)
    gram_part = owner_sums(zed, zed)
    gram = jnp.sum(lax.all_to_all(gram_part, "tile", 0, 0, tiled=True), axis=0)
    factor = jnp.linalg.cholesky((members - 1.0) * eye + gram)
    partner_factor = from_partner(factor, "half", 0)
    ens_f = ensemble[0].astype(jnp.float32)
    center = jnp.mean(ens_f, axis=1, keepdims=True)
    anomalies = (ens_f - center).astype(jnp.bfloat16)
    anomalies, partner_zed, partner_factor = lax.optimization_barrier((anomalies, partner_zed, partner_factor))
    partner_anom = from_partner(anomalies, "half", 0)

    cross_part = owner_sums(partner_zed, unn).astype(jnp.bfloat16)
    cross = jnp.sum(lax.all_to_all(cross_part, "tile", 0, 0, tiled=True), axis=0, dtype=jnp.float32)
    weights = jax.scipy.linalg.cho_solve((partner_factor, True), cross)
    loc_row = jnp.sum(
        loc_weight[0][:, None] * (neighbours[0][:, None] == tile_ids[None, :]).astype(jnp.float32),
        axis=0,
    )
    reach = (loc_row[:, None, None] * weights[None, :, :]).astype(jnp.bfloat16)
    got = lax.all_to_all(reach, "tile", 0, 0, tiled=True)
    spread = jnp.sum(got, axis=0, dtype=jnp.float32).astype(jnp.bfloat16)
    incr = jnp.dot(partner_anom, spread, preferred_element_type=jnp.float32).astype(jnp.bfloat16)
    analysis = (ens_f + incr.astype(jnp.float32)).astype(jnp.bfloat16)
    return analysis[None]


def solution(mesh):
    return jax.shard_map(
        step,
        mesh=mesh,
        in_specs=(
            P("half", "tile", None),
            P("half", "tile", None),
            P("tile"),
            P("tile", None),
            P("tile"),
            P("tile", None),
            P("tile", None),
            P("half", "tile", None),
        ),
        out_specs=P("half", "tile", None),
        check_vma=False,
    )
```

```python
import jax
import jax.numpy as jnp
from jax import lax
from jax.sharding import PartitionSpec as P


def from_partner(block, axis, apart):
    count = lax.axis_size(axis)
    route = []
    for low in range(count):
        high = low | 1 << apart
        if high != low and high < count:
            route += [(low, high), (high, low)]
    return lax.ppermute(block, axis, route)


def step(innov, pred, obs_weight, owner, counts, neighbours, loc_weight, ensemble):
    tiles = lax.axis_size("tile")
    members = pred.shape[2]
    obs_rows = pred.shape[1]
    blocks = owner.shape[0]
    block_rows = obs_rows // blocks
    block_ids = jnp.arange(blocks, dtype=jnp.int32)
    live = (block_ids < counts[0]).astype(jnp.float32)
    row_scale = obs_weight * jnp.repeat(live, block_rows)
    zed = (pred[0].astype(jnp.float32) * row_scale[:, None]).astype(jnp.bfloat16)
    unn = (innov[0].astype(jnp.float32) * row_scale[:, None]).astype(jnp.bfloat16)
    partner_pred = from_partner(pred[0], "half", 0)

    dest = owner[:, 0]
    tile_ids = jnp.arange(tiles, dtype=jnp.int32)
    owned = (dest[None, :] == tile_ids[:, None]).astype(jnp.float32)

    def owner_sums(left, right):
        per_block = lax.dot_general(
            left.reshape(blocks, block_rows, members),
            right.reshape(blocks, block_rows, members),
            (((1,), (1,)), ((0,), (0,))),
            preferred_element_type=jnp.float32,
        )
        return lax.dot_general(owned, per_block, (((1,), (0,)), ((), ())), precision=lax.Precision.HIGHEST)

    eye = jnp.eye(members, dtype=jnp.float32)
    gram_part = owner_sums(zed, zed)
    gram = jnp.sum(lax.all_to_all(gram_part, "tile", 0, 0, tiled=True), axis=0)
    partner_gram = from_partner(gram, "half", 0)
    ens_f = ensemble[0].astype(jnp.float32)
    center = jnp.mean(ens_f, axis=1, keepdims=True)
    anomalies = (ens_f - center).astype(jnp.bfloat16)
    anomalies, partner_pred = lax.optimization_barrier((anomalies, partner_pred))
    partner_anom = from_partner(anomalies, "half", 0)

    partner_zed = (partner_pred.astype(jnp.float32) * row_scale[:, None]).astype(jnp.bfloat16)
    cross_part = owner_sums(partner_zed, unn).astype(jnp.bfloat16)
    cross = jnp.sum(lax.all_to_all(cross_part, "tile", 0, 0, tiled=True), axis=0, dtype=jnp.float32)
    factor = jnp.linalg.cholesky((members - 1.0) * eye + partner_gram)
    weights = jax.scipy.linalg.cho_solve((factor, True), cross)
    loc_row = jnp.sum(
        loc_weight[0][:, None] * (neighbours[0][:, None] == tile_ids[None, :]).astype(jnp.float32),
        axis=0,
    )
    reach = (loc_row[:, None, None] * weights[None, :, :]).astype(jnp.bfloat16)
    got = lax.all_to_all(reach, "tile", 0, 0, tiled=True)
    spread = jnp.sum(got, axis=0, dtype=jnp.float32).astype(jnp.bfloat16)
    incr = jnp.dot(partner_anom, spread, preferred_element_type=jnp.float32).astype(jnp.bfloat16)
    analysis = (ens_f + incr.astype(jnp.float32)).astype(jnp.bfloat16)
    return analysis[None]


def solution(mesh):
    return jax.shard_map(
        step,
        mesh=mesh,
        in_specs=(
            P("half", "tile", None),
            P("half", "tile", None),
            P("tile"),
            P("tile", None),
            P("tile"),
            P("tile", None),
            P("tile", None),
            P("half", "tile", None),
        ),
        out_specs=P("half", "tile", None),
        check_vma=False,
    )
```

```python
import jax
import jax.numpy as jnp
from jax import lax
from jax.sharding import PartitionSpec as P


def from_partner(block, axis, apart):
    count = lax.axis_size(axis)
    route = []
    for low in range(count):
        high = low | 1 << apart
        if high != low and high < count:
            route += [(low, high), (high, low)]
    return lax.ppermute(block, axis, route)


def to_owners(parts, tiles, lane):
    groups = [[t for t in range(tiles) if (t // lane) % 2 == side] for side in range(2)]
    rows = parts.shape[1]
    pairs = parts.reshape((tiles // 2, 2 * rows) + parts.shape[2:])
    got = lax.all_to_all(pairs, "tile", 0, 0, tiled=True, axis_index_groups=groups)
    both = jnp.sum(got, axis=0, dtype=jnp.float32)
    side = (lax.axis_index("tile") // lane) % 2
    mine = jnp.where(side == 0, both[:rows], both[rows:])
    theirs = jnp.where(side == 0, both[rows:], both[:rows])
    back = lax.ppermute(theirs, "tile", [(t, t ^ lane) for t in range(tiles)])
    return mine + back


def step(innov, pred, obs_weight, owner, counts, neighbours, loc_weight, ensemble):
    tiles = lax.axis_size("tile")
    members = pred.shape[2]
    obs_rows = pred.shape[1]
    blocks = owner.shape[0]
    block_rows = obs_rows // blocks
    block_ids = jnp.arange(blocks, dtype=jnp.int32)
    live = (block_ids < counts[0]).astype(jnp.float32)
    row_scale = obs_weight * jnp.repeat(live, block_rows)
    zed = (pred[0].astype(jnp.float32) * row_scale[:, None]).astype(jnp.bfloat16)
    unn = (innov[0].astype(jnp.float32) * row_scale[:, None]).astype(jnp.bfloat16)
    partner_pred = from_partner(pred[0], "half", 0)

    dest = owner[:, 0]
    tile_ids = jnp.arange(tiles, dtype=jnp.int32)
    lane = tiles // 8
    row_tile = (tile_ids // (2 * lane)) * (2 * lane) + (tile_ids % 2) * lane + (tile_ids // 2) % lane
    owned = (dest[None, :] == row_tile[:, None]).astype(jnp.float32)

    def owner_sums(left, right):
        per_block = lax.dot_general(
            left.reshape(blocks, block_rows, members),
            right.reshape(blocks, block_rows, members),
            (((1,), (1,)), ((0,), (0,))),
            preferred_element_type=jnp.float32,
        )
        return lax.dot_general(owned, per_block, (((1,), (0,)), ((), ())), precision=lax.Precision.HIGHEST)

    eye = jnp.eye(members, dtype=jnp.float32)
    gram_part = owner_sums(zed, zed)
    gram = to_owners(gram_part, tiles, lane)
    partner_gram = from_partner(gram, "half", 0)
    ens_f = ensemble[0].astype(jnp.float32)
    center = jnp.mean(ens_f, axis=1, keepdims=True)
    anomalies = (ens_f - center).astype(jnp.bfloat16)
    anomalies, partner_pred = lax.optimization_barrier((anomalies, partner_pred))
    partner_anom = from_partner(anomalies, "half", 0)

    partner_zed = (partner_pred.astype(jnp.float32) * row_scale[:, None]).astype(jnp.bfloat16)
    cross_part = owner_sums(partner_zed, unn)
    cross = to_owners(cross_part, tiles, lane)
    factor = jnp.linalg.cholesky((members - 1.0) * eye + partner_gram)
    weights = jax.scipy.linalg.cho_solve((factor, True), cross)
    loc_row = jnp.sum(
        loc_weight[0][:, None] * (neighbours[0][:, None] == tile_ids[None, :]).astype(jnp.float32),
        axis=0,
    )
    reach = loc_row[row_tile][:, None, None] * weights[None, :, :]
    spread = to_owners(reach, tiles, lane).astype(jnp.bfloat16)
    incr = jnp.dot(partner_anom, spread, preferred_element_type=jnp.float32).astype(jnp.bfloat16)
    analysis = (ens_f + incr.astype(jnp.float32)).astype(jnp.bfloat16)
    return analysis[None]


def solution(mesh):
    return jax.shard_map(
        step,
        mesh=mesh,
        in_specs=(
            P("half", "tile", None),
            P("half", "tile", None),
            P("tile"),
            P("tile", None),
            P("tile"),
            P("tile", None),
            P("tile", None),
            P("half", "tile", None),
        ),
        out_specs=P("half", "tile", None),
        check_vma=False,
    )
```

```python
import jax
import jax.numpy as jnp
from jax import lax
from jax.sharding import PartitionSpec as P


def from_partner(block, axis, apart):
    count = lax.axis_size(axis)
    route = []
    for low in range(count):
        high = low | 1 << apart
        if high != low and high < count:
            route += [(low, high), (high, low)]
    return lax.ppermute(block, axis, route)


def to_owners(parts, tiles, lane):
    groups = [[t for t in range(tiles) if (t // lane) % 2 == side] for side in range(2)]
    rows = parts.shape[1]
    pairs = parts.reshape((tiles // 2, 2 * rows) + parts.shape[2:])
    got = lax.all_to_all(pairs, "tile", 0, 0, tiled=True, axis_index_groups=groups)
    both = jnp.sum(got, axis=0, dtype=jnp.float32)
    side = (lax.axis_index("tile") // lane) % 2
    mine = jnp.where(side == 0, both[:rows], both[rows:])
    theirs = jnp.where(side == 0, both[rows:], both[:rows])
    back = lax.ppermute(theirs, "tile", [(t, t ^ lane) for t in range(tiles)])
    return mine + back


def spread_of(weights, loc_all, tiles, lane):
    half_count = tiles // 2
    groups = [[t for t in range(tiles) if (t // lane) % 2 == side] for side in range(2)]
    got = lax.all_to_all(
        jnp.broadcast_to(weights[None], (half_count,) + weights.shape), "tile", 0, 0, tiled=True, axis_index_groups=groups
    )
    me = lax.axis_index("tile")
    side = (me // lane) % 2
    slot = jnp.arange(half_count, dtype=jnp.int32)
    senders = (slot // lane) * (2 * lane) + side * lane + slot % lane
    column = me - side * lane
    takers = column + jnp.arange(2, dtype=jnp.int32) * lane
    coef = loc_all[senders[:, None], takers[None, :]]
    both = lax.dot_general(coef, got, (((0,), (0,)), ((), ())), precision=lax.Precision.HIGHEST)
    mine = jnp.where(side == 0, both[0], both[1])
    theirs = jnp.where(side == 0, both[1], both[0])
    back = lax.ppermute(theirs, "tile", [(t, t ^ lane) for t in range(tiles)])
    return mine + back


def step(innov, pred, obs_weight, owner, counts, neighbours, loc_weight, ensemble):
    tiles = lax.axis_size("tile")
    members = pred.shape[2]
    obs_rows = pred.shape[1]
    blocks = owner.shape[0]
    block_rows = obs_rows // blocks
    block_ids = jnp.arange(blocks, dtype=jnp.int32)
    live = (block_ids < counts[0]).astype(jnp.float32)
    row_scale = obs_weight * jnp.repeat(live, block_rows)
    zed = (pred[0].astype(jnp.float32) * row_scale[:, None]).astype(jnp.bfloat16)
    unn = (innov[0].astype(jnp.float32) * row_scale[:, None]).astype(jnp.bfloat16)
    partner_pred = from_partner(pred[0], "half", 0)

    dest = owner[:, 0]
    tile_ids = jnp.arange(tiles, dtype=jnp.int32)
    lane = tiles // 8
    row_tile = (tile_ids // (2 * lane)) * (2 * lane) + (tile_ids % 2) * lane + (tile_ids // 2) % lane
    owned = (dest[None, :] == row_tile[:, None]).astype(jnp.float32)

    def owner_sums(left, right):
        per_block = lax.dot_general(
            left.reshape(blocks, block_rows, members),
            right.reshape(blocks, block_rows, members),
            (((1,), (1,)), ((0,), (0,))),
            preferred_element_type=jnp.float32,
        )
        return lax.dot_general(owned, per_block, (((1,), (0,)), ((), ())), precision=lax.Precision.HIGHEST)

    eye = jnp.eye(members, dtype=jnp.float32)
    gram_part = owner_sums(zed, zed)
    loc_row = jnp.sum(
        loc_weight[0][:, None] * (neighbours[0][:, None] == tile_ids[None, :]).astype(jnp.float32),
        axis=0,
    )
    loc_all = lax.all_gather(loc_row, "tile")
    gram_part, loc_all = lax.optimization_barrier((gram_part, loc_all))
    gram = to_owners(gram_part, tiles, lane)
    partner_gram = from_partner(gram, "half", 0)
    ens_f = ensemble[0].astype(jnp.float32)
    center = jnp.mean(ens_f, axis=1, keepdims=True)
    anomalies = (ens_f - center).astype(jnp.bfloat16)
    anomalies, partner_pred = lax.optimization_barrier((anomalies, partner_pred))
    partner_anom = from_partner(anomalies, "half", 0)

    partner_zed = (partner_pred.astype(jnp.float32) * row_scale[:, None]).astype(jnp.bfloat16)
    cross_part = owner_sums(partner_zed, unn)
    cross = to_owners(cross_part, tiles, lane)
    factor = jnp.linalg.cholesky((members - 1.0) * eye + partner_gram)
    weights = jax.scipy.linalg.cho_solve((factor, True), cross)
    spread = spread_of(weights, loc_all, tiles, lane).astype(jnp.bfloat16)
    incr = jnp.dot(partner_anom, spread, preferred_element_type=jnp.float32).astype(jnp.bfloat16)
    analysis = (ens_f + incr.astype(jnp.float32)).astype(jnp.bfloat16)
    return analysis[None]


def solution(mesh):
    return jax.shard_map(
        step,
        mesh=mesh,
        in_specs=(
            P("half", "tile", None),
            P("half", "tile", None),
            P("tile"),
            P("tile", None),
            P("tile"),
            P("tile", None),
            P("tile", None),
            P("half", "tile", None),
        ),
        out_specs=P("half", "tile", None),
        check_vma=False,
    )
```

```python
import jax
import jax.numpy as jnp
from jax import lax
from jax.sharding import PartitionSpec as P


def from_partner(block, axis, apart):
    count = lax.axis_size(axis)
    route = []
    for low in range(count):
        high = low | 1 << apart
        if high != low and high < count:
            route += [(low, high), (high, low)]
    return lax.ppermute(block, axis, route)


def to_owners(parts, tiles, lane):
    groups = [[t for t in range(tiles) if (t // lane) % 2 == side] for side in range(2)]
    rows = parts.shape[1]
    pairs = parts.reshape((tiles // 2, 2 * rows) + parts.shape[2:])
    got = lax.all_to_all(pairs, "tile", 0, 0, tiled=True, axis_index_groups=groups)
    both = jnp.sum(got, axis=0, dtype=jnp.float32)
    side = (lax.axis_index("tile") // lane) % 2
    mine = jnp.where(side == 0, both[:rows], both[rows:])
    theirs = jnp.where(side == 0, both[rows:], both[:rows])
    back = lax.ppermute(theirs, "tile", [(t, t ^ lane) for t in range(tiles)])
    return mine + back


def spread_of(weights, loc_pairs, tiles, lane):
    half_count = tiles // 2
    members = weights.shape[1]
    groups = [[t for t in range(tiles) if (t // lane) % 2 == side] for side in range(2)]
    extra = jnp.zeros((half_count, 8, members), jnp.float32).at[:, 0, :2].set(loc_pairs.reshape(half_count, 2))
    sent = jnp.concatenate([jnp.broadcast_to(weights[None], (half_count,) + weights.shape), extra], axis=1)
    got = lax.all_to_all(sent, "tile", 0, 0, tiled=True, axis_index_groups=groups)
    coef = got[:, weights.shape[0], :2]
    both = lax.dot_general(coef, got[:, : weights.shape[0]], (((0,), (0,)), ((), ())), precision=lax.Precision.HIGHEST)
    side = (lax.axis_index("tile") // lane) % 2
    mine = jnp.where(side == 0, both[0], both[1])
    theirs = jnp.where(side == 0, both[1], both[0])
    back = lax.ppermute(theirs, "tile", [(t, t ^ lane) for t in range(tiles)])
    return mine + back


def step(innov, pred, obs_weight, owner, counts, neighbours, loc_weight, ensemble):
    tiles = lax.axis_size("tile")
    members = pred.shape[2]
    obs_rows = pred.shape[1]
    blocks = owner.shape[0]
    block_rows = obs_rows // blocks
    block_ids = jnp.arange(blocks, dtype=jnp.int32)
    live = (block_ids < counts[0]).astype(jnp.float32)
    row_scale = obs_weight * jnp.repeat(live, block_rows)
    zed = (pred[0].astype(jnp.float32) * row_scale[:, None]).astype(jnp.bfloat16)
    unn = (innov[0].astype(jnp.float32) * row_scale[:, None]).astype(jnp.bfloat16)
    partner_pred = from_partner(pred[0], "half", 0)

    dest = owner[:, 0]
    tile_ids = jnp.arange(tiles, dtype=jnp.int32)
    lane = tiles // 8
    row_tile = (tile_ids // (2 * lane)) * (2 * lane) + (tile_ids % 2) * lane + (tile_ids // 2) % lane
    owned = (dest[None, :] == row_tile[:, None]).astype(jnp.float32)

    def owner_sums(left, right):
        per_block = lax.dot_general(
            left.reshape(blocks, block_rows, members),
            right.reshape(blocks, block_rows, members),
            (((1,), (1,)), ((0,), (0,))),
            preferred_element_type=jnp.float32,
        )
        return lax.dot_general(owned, per_block, (((1,), (0,)), ((), ())), precision=lax.Precision.HIGHEST)

    eye = jnp.eye(members, dtype=jnp.float32)
    gram_part = owner_sums(zed, zed)
    loc_row = jnp.sum(
        loc_weight[0][:, None] * (neighbours[0][:, None] == tile_ids[None, :]).astype(jnp.float32),
        axis=0,
    )
    gram = to_owners(gram_part, tiles, lane)
    partner_gram = from_partner(gram, "half", 0)
    ens_f = ensemble[0].astype(jnp.float32)
    center = jnp.mean(ens_f, axis=1, keepdims=True)
    anomalies = (ens_f - center).astype(jnp.bfloat16)
    anomalies, partner_pred = lax.optimization_barrier((anomalies, partner_pred))
    partner_anom = from_partner(anomalies, "half", 0)

    partner_zed = (partner_pred.astype(jnp.float32) * row_scale[:, None]).astype(jnp.bfloat16)
    cross_part = owner_sums(partner_zed, unn)
    cross = to_owners(cross_part, tiles, lane)
    factor = jnp.linalg.cholesky((members - 1.0) * eye + partner_gram)
    weights = jax.scipy.linalg.cho_solve((factor, True), cross)
    spread = spread_of(weights, loc_row[row_tile], tiles, lane).astype(jnp.bfloat16)
    incr = jnp.dot(partner_anom, spread, preferred_element_type=jnp.float32).astype(jnp.bfloat16)
    analysis = (ens_f + incr.astype(jnp.float32)).astype(jnp.bfloat16)
    return analysis[None]


def solution(mesh):
    return jax.shard_map(
        step,
        mesh=mesh,
        in_specs=(
            P("half", "tile", None),
            P("half", "tile", None),
            P("tile"),
            P("tile", None),
            P("tile"),
            P("tile", None),
            P("tile", None),
            P("half", "tile", None),
        ),
        out_specs=P("half", "tile", None),
        check_vma=False,
    )
```

```python
import jax
import jax.numpy as jnp
from jax import lax
from jax.sharding import PartitionSpec as P


def from_partner(block, axis, apart):
    count = lax.axis_size(axis)
    route = []
    for low in range(count):
        high = low | 1 << apart
        if high != low and high < count:
            route += [(low, high), (high, low)]
    return lax.ppermute(block, axis, route)


def to_owners(parts, tiles, lane):
    groups = [[t for t in range(tiles) if (t // lane) % 2 == side] for side in range(2)]
    rows = parts.shape[1]
    pairs = parts.reshape((tiles // 2, 2 * rows) + parts.shape[2:])
    got = lax.all_to_all(pairs, "tile", 0, 0, tiled=True, axis_index_groups=groups)
    both = jnp.sum(got, axis=0, dtype=jnp.float32)
    side = (lax.axis_index("tile") // lane) % 2
    mine = jnp.where(side == 0, both[:rows], both[rows:])
    theirs = jnp.where(side == 0, both[rows:], both[:rows])
    back = lax.ppermute(theirs, "tile", [(t, t ^ lane) for t in range(tiles)])
    return mine + back


def spread_of(weights, loc_pairs, tiles, lane):
    half_count = tiles // 2
    members = weights.shape[1]
    groups = [[t for t in range(tiles) if (t // lane) % 2 == side] for side in range(2)]
    extra = jnp.zeros((half_count, 8, members), jnp.float32).at[:, 0, :2].set(loc_pairs.reshape(half_count, 2))
    sent = jnp.concatenate([jnp.broadcast_to(weights[None], (half_count,) + weights.shape), extra], axis=1)
    got = lax.all_to_all(sent, "tile", 0, 0, tiled=True, axis_index_groups=groups)
    coef = got[:, weights.shape[0], :2]
    both = lax.dot_general(coef, got[:, : weights.shape[0]], (((0,), (0,)), ((), ())), precision=lax.Precision.HIGHEST)
    side = (lax.axis_index("tile") // lane) % 2
    mine = jnp.where(side == 0, both[0], both[1])
    theirs = jnp.where(side == 0, both[1], both[0])
    back = lax.ppermute(theirs, "tile", [(t, t ^ lane) for t in range(tiles)])
    return mine + back


def step(innov, pred, obs_weight, owner, counts, neighbours, loc_weight, ensemble):
    tiles = lax.axis_size("tile")
    members = pred.shape[2]
    obs_rows = pred.shape[1]
    blocks = owner.shape[0]
    block_rows = obs_rows // blocks
    block_ids = jnp.arange(blocks, dtype=jnp.int32)
    live = (block_ids < counts[0]).astype(jnp.float32)
    row_scale = obs_weight * jnp.repeat(live, block_rows)
    zed = (pred[0].astype(jnp.float32) * row_scale[:, None]).astype(jnp.bfloat16)
    unn = (innov[0].astype(jnp.float32) * row_scale[:, None]).astype(jnp.bfloat16)
    split = obs_rows // 2
    partner_head = from_partner(pred[0][:split], "half", 0)
    partner_tail = from_partner(pred[0][split:], "half", 0)

    dest = owner[:, 0]
    tile_ids = jnp.arange(tiles, dtype=jnp.int32)
    lane = tiles // 8
    row_tile = (tile_ids // (2 * lane)) * (2 * lane) + (tile_ids % 2) * lane + (tile_ids // 2) % lane
    owned = (dest[None, :] == row_tile[:, None]).astype(jnp.float32)

    def owner_sums(left, right, owned=owned):
        count = left.shape[0] // block_rows
        per_block = lax.dot_general(
            left.reshape(count, block_rows, members),
            right.reshape(count, block_rows, members),
            (((1,), (1,)), ((0,), (0,))),
            preferred_element_type=jnp.float32,
        )
        return lax.dot_general(owned, per_block, (((1,), (0,)), ((), ())), precision=lax.Precision.HIGHEST)

    eye = jnp.eye(members, dtype=jnp.float32)
    gram_part = owner_sums(zed, zed)
    loc_row = jnp.sum(
        loc_weight[0][:, None] * (neighbours[0][:, None] == tile_ids[None, :]).astype(jnp.float32),
        axis=0,
    )
    gram = to_owners(gram_part, tiles, lane)
    partner_gram = from_partner(gram, "half", 0)
    ens_f = ensemble[0].astype(jnp.float32)
    center = jnp.mean(ens_f, axis=1, keepdims=True)
    anomalies = (ens_f - center).astype(jnp.bfloat16)
    anomalies, partner_tail = lax.optimization_barrier((anomalies, partner_tail))
    partner_anom = from_partner(anomalies, "half", 0)

    head_blocks = split // block_rows
    head_zed = (partner_head.astype(jnp.float32) * row_scale[:split, None]).astype(jnp.bfloat16)
    head_part = owner_sums(head_zed, unn[:split], owned[:, :head_blocks])
    tail_zed = (partner_tail.astype(jnp.float32) * row_scale[split:, None]).astype(jnp.bfloat16)
    cross_part = head_part + owner_sums(tail_zed, unn[split:], owned[:, head_blocks:])
    cross = to_owners(cross_part, tiles, lane)
    factor = jnp.linalg.cholesky((members - 1.0) * eye + partner_gram)
    weights = jax.scipy.linalg.cho_solve((factor, True), cross)
    spread = spread_of(weights, loc_row[row_tile], tiles, lane).astype(jnp.bfloat16)
    incr = jnp.dot(partner_anom, spread, preferred_element_type=jnp.float32).astype(jnp.bfloat16)
    analysis = (ens_f + incr.astype(jnp.float32)).astype(jnp.bfloat16)
    return analysis[None]


def solution(mesh):
    return jax.shard_map(
        step,
        mesh=mesh,
        in_specs=(
            P("half", "tile", None),
            P("half", "tile", None),
            P("tile"),
            P("tile", None),
            P("tile"),
            P("tile", None),
            P("tile", None),
            P("half", "tile", None),
        ),
        out_specs=P("half", "tile", None),
        check_vma=False,
    )
```

```python
import jax
import jax.numpy as jnp
from jax import lax
from jax.sharding import PartitionSpec as P


def from_partner(block, axis, apart):
    count = lax.axis_size(axis)
    route = []
    for low in range(count):
        high = low | 1 << apart
        if high != low and high < count:
            route += [(low, high), (high, low)]
    return lax.ppermute(block, axis, route)


def to_owners(parts, tiles, lane):
    groups = [[t for t in range(tiles) if (t // lane) % 2 == side] for side in range(2)]
    rows = parts.shape[1]
    pairs = parts.reshape((tiles // 2, 2 * rows) + parts.shape[2:])
    got = lax.all_to_all(pairs, "tile", 0, 0, tiled=True, axis_index_groups=groups)
    both = jnp.sum(got, axis=0, dtype=jnp.float32)
    side = (lax.axis_index("tile") // lane) % 2
    mine = jnp.where(side == 0, both[:rows], both[rows:])
    theirs = jnp.where(side == 0, both[rows:], both[:rows])
    back = lax.ppermute(theirs, "tile", [(t, t ^ lane) for t in range(tiles)])
    return mine + back


def spread_of(weights, loc_pairs, tiles, lane):
    half_count = tiles // 2
    members = weights.shape[1]
    groups = [[t for t in range(tiles) if (t // lane) % 2 == side] for side in range(2)]
    extra = jnp.zeros((half_count, 8, members), jnp.float32).at[:, 0, :2].set(loc_pairs.reshape(half_count, 2))
    sent = jnp.concatenate([jnp.broadcast_to(weights[None], (half_count,) + weights.shape), extra], axis=1)
    got = lax.all_to_all(sent, "tile", 0, 0, tiled=True, axis_index_groups=groups)
    coef = got[:, weights.shape[0], :2]
    both = jnp.sum(coef.T[:, :, None, None] * got[None, :, : weights.shape[0]], axis=1)
    side = (lax.axis_index("tile") // lane) % 2
    mine = jnp.where(side == 0, both[0], both[1])
    theirs = jnp.where(side == 0, both[1], both[0])
    back = lax.ppermute(theirs, "tile", [(t, t ^ lane) for t in range(tiles)])
    return mine + back


def step(innov, pred, obs_weight, owner, counts, neighbours, loc_weight, ensemble):
    tiles = lax.axis_size("tile")
    members = pred.shape[2]
    obs_rows = pred.shape[1]
    blocks = owner.shape[0]
    block_rows = obs_rows // blocks
    block_ids = jnp.arange(blocks, dtype=jnp.int32)
    live = (block_ids < counts[0]).astype(jnp.float32)
    row_scale = obs_weight * jnp.repeat(live, block_rows)
    zed = (pred[0].astype(jnp.float32) * row_scale[:, None]).astype(jnp.bfloat16)
    unn = (innov[0].astype(jnp.float32) * row_scale[:, None]).astype(jnp.bfloat16)
    split = obs_rows // 2
    partner_head = from_partner(pred[0][:split], "half", 0)
    partner_tail = from_partner(pred[0][split:], "half", 0)

    dest = owner[:, 0]
    tile_ids = jnp.arange(tiles, dtype=jnp.int32)
    lane = tiles // 8
    row_tile = (tile_ids // (2 * lane)) * (2 * lane) + (tile_ids % 2) * lane + (tile_ids // 2) % lane
    owned = (dest[None, :] == row_tile[:, None]).astype(jnp.float32)

    def owner_sums(left, right, owned=owned):
        count = left.shape[0] // block_rows
        per_block = lax.dot_general(
            left.reshape(count, block_rows, members),
            right.reshape(count, block_rows, members),
            (((1,), (1,)), ((0,), (0,))),
            preferred_element_type=jnp.float32,
        )
        return lax.dot_general(owned, per_block, (((1,), (0,)), ((), ())), precision=lax.Precision.HIGHEST)

    eye = jnp.eye(members, dtype=jnp.float32)
    gram_part = owner_sums(zed, zed)
    loc_row = jnp.sum(
        loc_weight[0][:, None] * (neighbours[0][:, None] == tile_ids[None, :]).astype(jnp.float32),
        axis=0,
    )
    gram = to_owners(gram_part, tiles, lane)
    partner_gram = from_partner(gram, "half", 0)
    ens_f = ensemble[0].astype(jnp.float32)
    center = jnp.mean(ens_f, axis=1, keepdims=True)
    anomalies = (ens_f - center).astype(jnp.bfloat16)
    anomalies, partner_tail = lax.optimization_barrier((anomalies, partner_tail))
    partner_anom_head = from_partner(anomalies[:split], "half", 0)

    head_blocks = split // block_rows
    head_zed = (partner_head.astype(jnp.float32) * row_scale[:split, None]).astype(jnp.bfloat16)
    head_part = owner_sums(head_zed, unn[:split], owned[:, :head_blocks])
    tail_zed = (partner_tail.astype(jnp.float32) * row_scale[split:, None]).astype(jnp.bfloat16)
    cross_part = head_part + owner_sums(tail_zed, unn[split:], owned[:, head_blocks:])
    cross = to_owners(cross_part, tiles, lane)
    anom_tail, cross = lax.optimization_barrier((anomalies[split:], cross))
    partner_anom_tail = from_partner(anom_tail, "half", 0)
    factor = jnp.linalg.cholesky((members - 1.0) * eye + partner_gram)
    weights = jax.scipy.linalg.cho_solve((factor, True), cross)
    spread = spread_of(weights, loc_row[row_tile], tiles, lane).astype(jnp.bfloat16)
    partner_anom = jnp.concatenate([partner_anom_head, partner_anom_tail], axis=0)
    incr = jnp.dot(partner_anom, spread, preferred_element_type=jnp.float32).astype(jnp.bfloat16)
    analysis = (ens_f + incr.astype(jnp.float32)).astype(jnp.bfloat16)
    return analysis[None]


def solution(mesh):
    return jax.shard_map(
        step,
        mesh=mesh,
        in_specs=(
            P("half", "tile", None),
            P("half", "tile", None),
            P("tile"),
            P("tile", None),
            P("tile"),
            P("tile", None),
            P("tile", None),
            P("half", "tile", None),
        ),
        out_specs=P("half", "tile", None),
        check_vma=False,
    )
```
